256 devices in a mesh: layer: 32 (over z, y), fblk: 8 (over x, core).
Axes of the slice: x: 4, y: 4, z: 8, core: 2. Of those that a mesh axis runs over, the one named last changes fastest.
Arguments:
- decoder: bfloat16 [4608, 131072], P('fblk', 'layer'), may hold values from -0.09375 to 0.09375
- encoder: bfloat16 [4608, 131072], P('fblk', 'layer'), may hold values from -0.09375 to 0.09375
- activation: bfloat16 [4, 131072], P(None, 'layer'), may hold values from 0.29882812 to 3
- blocks: int32 [4, 9, 3], replicated, may hold values from 0 to 31, as said below
- counts: int32 [4, 9], replicated, may hold values from 1 to 3
Outputs:
- influence: bfloat16 [32, 1536, 1536], P('layer', 'fblk')
The draws below stay inside these ranges and needn't reach their ends.
Inputs may be any that keep to these rules, and one draw needn't show every extreme that they name: `blocks`: the 3 block numbers of one prompt and layer are distinct.
All inputs are finite; a program needn't handle non-finite values.
Results may differ from the reference program's by a relative error of at most 0.038.
Values may be sent and summed in bfloat16 or wider, within the bound.
No kernel may reach another device: no remote copies, remote signals or barrier semaphores. Data moves between devices by JAX's collectives and lax.ppermute only.
A program may use at most 128 MiB of HBM per device.

```python
import math
import jax
import jax.numpy as jnp
from jax import lax

D = 4608
FEAT = 16384
BLK = 512
ACTIVE_SLOTS = 3
LAYERS = 8
PROMPTS = 4
FEATURE_BLOCKS = 32
N_FBLK = 8


def draw_blocks(key, part):
    score_key = jax.random.fold_in(key, 11)
    first_key = jax.random.fold_in(key, 12)
    second_key = jax.random.fold_in(key, 13)
    block_scores = jax.random.randint(score_key, (PROMPTS, LAYERS + 1, FEATURE_BLOCKS), 0, 1 << 20) * FEATURE_BLOCKS
    block_scores = block_scores + jnp.arange(FEATURE_BLOCKS, dtype=jnp.int32)[None, None, :]
    row_positions = jnp.arange(PROMPTS * (LAYERS + 1), dtype=jnp.int32).reshape(PROMPTS, LAYERS + 1)
    highest_row = jax.random.randint(first_key, (), 0, PROMPTS * (LAYERS + 1))
    lowest_row = jax.random.randint(second_key, (), 0, PROMPTS * (LAYERS + 1))
    column_positions = jnp.arange(FEATURE_BLOCKS, dtype=jnp.int32)[None, None, :]
    extra_score = jnp.where((row_positions == highest_row)[:, :, None] & (column_positions == FEATURE_BLOCKS - 1), 1 << 26, 0)
    extra_score = extra_score + jnp.where((row_positions == lowest_row)[:, :, None] & (column_positions == 0), 1 << 26, 0)
    value_entries, picked_blocks = lax.top_k(block_scores + extra_score, ACTIVE_SLOTS)
    return picked_blocks.astype(jnp.int32)


def place_ends(entries, own_key, smallest, high):
    longest = entries.shape.index(max(entries.shape))
    spots = []
    for shift in (0, 1):
        where = [jax.random.randint(jax.random.fold_in(own_key, axis), (), 0, length) for axis, length in enumerate(entries.shape)]
        where[longest] = (where[longest] + shift) % entries.shape[longest]
        spots.append(tuple(where))
    return entries.at[spots[0]].set(smallest).at[spots[1]].set(high)


def steps_of(stream_key, dims, split, low, high):
    def one(position, blocks):
        draws = jax.random.uniform(jax.random.fold_in(jax.random.fold_in(stream_key, 6), position), (blocks,), jnp.float32, low / len(split), high / len(split))
        return jnp.repeat(jnp.exp(draws), dims[position] // blocks).reshape((-1,) + (1,) * (len(dims) - position - 1))

    factor_of = one(*split[0])
    for cut in split[1:]:
        factor_of = factor_of * one(*cut)
    return factor_of


def noise(own_key, shape, spread, reach, split=(), kind=jnp.bfloat16):
    drawn = spread * jax.random.normal(own_key, shape, jnp.float32)
    if split:
        drawn = drawn * steps_of(own_key, shape, split, -0.22, 0.18)
    return jnp.clip(drawn, -reach, reach).astype(kind)


def setup_inputs(seed: int = 0) -> dict:
    arg_keys = jax.random.split(jax.random.key(seed), 6)
    decoder = noise(arg_keys[0], (D, LAYERS * FEAT), D ** -0.5, 0.09375, ((0, 8), (1, 32)))
    encoder = noise(arg_keys[1], (D, LAYERS * FEAT), D ** -0.5, 0.09375, ((0, 8), (1, 32)))
    activation = jnp.clip(jnp.exp(math.log(3.0) - 2.306499 * jax.random.uniform(arg_keys[2], (PROMPTS, LAYERS * FEAT), jnp.float32) ** steps_of(arg_keys[2], (PROMPTS, LAYERS * FEAT), ((1, 32),), -0.2, 0.2)), 0.29882812, 3.0).astype(jnp.bfloat16)
    blocks = draw_blocks(jax.random.fold_in(arg_keys[5], 71), 0)
    counts = place_ends(jax.random.randint(arg_keys[4], (PROMPTS, LAYERS + 1), 1, ACTIVE_SLOTS + 1), jax.random.fold_in(arg_keys[4], 1), 1, ACTIVE_SLOTS).astype(jnp.int32)
    return {"decoder": decoder, "encoder": encoder, "activation": activation, "blocks": blocks, "counts": counts}


def select_columns(matrix, layer_index, block_ids, active_count, weights):
    pieces = []
    for slot_index in range(ACTIVE_SLOTS):
        offset = (layer_index * FEAT + block_ids[slot_index] * BLK).astype(jnp.int32)
        column_block = lax.dynamic_slice_in_dim(matrix, offset, BLK, 1).astype(jnp.float32)
        if weights is not None:
            factor = lax.dynamic_slice_in_dim(weights, offset, BLK, 0).astype(jnp.float32)
            column_block = column_block * factor[None, :]
        pieces.append(jnp.where(slot_index < active_count, column_block, jnp.zeros_like(column_block)))
    return jnp.concatenate(pieces, 1).astype(jnp.bfloat16)

def reference(decoder, encoder, activation, blocks, counts):
    slice_width = D // N_FBLK
    results = {}
    for prompt in range(PROMPTS):
        product_chain = None
        for layer_index in range(LAYERS):
            source = select_columns(decoder, layer_index, blocks[prompt, layer_index], counts[prompt, layer_index], activation[prompt])
            target = select_columns(encoder, layer_index, blocks[prompt, layer_index + 1], counts[prompt, layer_index + 1], None)
            gram_sum = jnp.zeros((ACTIVE_SLOTS * BLK, ACTIVE_SLOTS * BLK), jnp.float32)
            for slice_index in range(N_FBLK):
                lower_row = slice_index * slice_width
                partial_value = jnp.dot(target[lower_row:lower_row + slice_width].T, source[lower_row:lower_row + slice_width], preferred_element_type=jnp.float32)
                rounded = lax.optimization_barrier(partial_value.astype(jnp.bfloat16))
                gram_sum = gram_sum + rounded.astype(jnp.float32)
            live_rows = (counts[prompt, layer_index] * BLK).astype(jnp.float32)
            row_mean = lax.optimization_barrier(jnp.sum(jnp.abs(gram_sum), axis=1)) / live_rows
            edges = (0.7 * gram_sum / ((row_mean[:, None] + 1e-06) * jnp.sqrt(live_rows))).astype(jnp.bfloat16)
            if layer_index == 0:
                product_chain = edges
            else:
                product_chain = jnp.dot(edges, product_chain, preferred_element_type=jnp.float32).astype(jnp.bfloat16)
            scaled = jnp.sqrt(jnp.float32(ACTIVE_SLOTS * BLK)) * product_chain.astype(jnp.float32)
            results[layer_index * PROMPTS + prompt] = scaled.astype(jnp.bfloat16)
    return jnp.stack([results[entry] for entry in range(LAYERS * PROMPTS)], 0)
```

```python
import jax
import jax.numpy as jnp
from jax import lax
from jax.sharding import Mesh
from jax.sharding import PartitionSpec as P

BLK = 512
ACTIVE_SLOTS = 3
LAYERS = 8


def pick_blocks(matrix, weights, block_ids, active_count, quarter, local_blocks):
    prompts, slots = block_ids.shape
    rows = matrix.shape[0]
    out = []
    for prompt in range(prompts):
        pieces = []
        for slot in range(slots):
            block = block_ids[prompt, slot]
            local = block % local_blocks
            live = (slot < active_count[prompt]) & (block // local_blocks == quarter)
            column_block = lax.dynamic_slice(matrix, (0, local * BLK), (rows, BLK)).astype(jnp.float32)
            if weights is not None:
                factor = lax.dynamic_slice(weights[prompt], (local * BLK,), (BLK,)).astype(jnp.float32)
                column_block = column_block * factor[None, :]
            pieces.append(jnp.where(live, column_block, 0.0).astype(jnp.bfloat16))
        out.append(jnp.concatenate(pieces, 1))
    return jnp.stack(out, 0)


def on_device(decoder, encoder, activation, blocks, counts):
    group_count = lax.axis_size("lg")
    layer_group = lax.axis_index("lg")
    quarter = lax.axis_index("q")
    fblk = lax.axis_index("fblk")
    fblk_count = lax.axis_size("fblk")
    slice_width, local_columns = decoder.shape
    local_blocks = local_columns // BLK
    active_width = ACTIVE_SLOTS * BLK
    column_share = active_width // fblk_count

    source_ids = lax.dynamic_index_in_dim(blocks, layer_group, 1, False)
    source_counts = lax.dynamic_index_in_dim(counts, layer_group, 1, False)
    target_ids = lax.dynamic_index_in_dim(blocks, layer_group + 1, 1, False)
    target_counts = lax.dynamic_index_in_dim(counts, layer_group + 1, 1, False)
    source = pick_blocks(decoder, activation, source_ids, source_counts, quarter, local_blocks)
    target = pick_blocks(encoder, None, target_ids, target_counts, quarter, local_blocks)
    combined = jnp.concatenate([source, target], axis=2)
    combined = lax.psum_scatter(combined, "q", scatter_dimension=0, tiled=True)
    source = combined[0, :, :active_width]
    target = combined[0, :, active_width:]

    partial_gram = lax.dot_general(
        target, source, (((0,), (0,)), ((), ())), preferred_element_type=jnp.float32
    ).astype(jnp.bfloat16)
    gram_sum = lax.psum(partial_gram, "fblk").astype(jnp.float32)
    live_rows = (lax.dynamic_slice(counts, (quarter, layer_group), (1, 1))[0, 0] * BLK).astype(
        jnp.float32
    )
    row_mean = jnp.sum(jnp.abs(gram_sum), axis=1) / live_rows
    edges = (0.7 * gram_sum / ((row_mean[:, None] + 1e-06) * jnp.sqrt(live_rows))).astype(
        jnp.bfloat16
    )

    chain = lax.dynamic_slice_in_dim(edges, fblk * column_share, column_share, 1)
    forward = [(index, index + 1) for index in range(group_count - 1)]
    for step in range(1, group_count):
        previous = lax.ppermute(chain, "lg", forward)
        product = jnp.dot(edges, previous, preferred_element_type=jnp.float32).astype(jnp.bfloat16)
        chain = jnp.where(layer_group == step, product, chain)
    rows = lax.all_to_all(chain, "fblk", 0, 1, tiled=True)
    influence = (jnp.sqrt(jnp.float32(active_width)) * rows.astype(jnp.float32)).astype(
        jnp.bfloat16
    )
    return influence[None]


def solution(mesh):
    layer_count = mesh.shape["layer"]
    fblk_count = mesh.shape["fblk"]
    split = Mesh(
        mesh.devices.reshape(LAYERS, layer_count // LAYERS, fblk_count), ("lg", "q", "fblk")
    )
    layer = ("lg", "q")
    in_specs = (P("fblk", layer), P("fblk", layer), P(None, layer), P(), P())
    out_specs = P(layer, "fblk", None)
    return jax.shard_map(
        on_device, mesh=split, in_specs=in_specs, out_specs=out_specs, check_vma=False
    )
```

```python
import jax
import jax.numpy as jnp
from jax import lax
from jax.experimental import pallas as pl
from jax.experimental.pallas import tpu as pltpu
from jax.sharding import Mesh
from jax.sharding import PartitionSpec as P

BLK = 512
ACTIVE_SLOTS = 3
LAYERS = 8
CHUNKS = 4


def select_kernel(src_loc, tgt_loc, src_live, tgt_live, dec_ref, enc_ref, act_ref, out_ref):
    prompt = pl.program_id(0)
    column = pl.program_id(1)

    @pl.when(column < ACTIVE_SLOTS)
    def _():
        weights = act_ref[...].astype(jnp.float32)
        row = lax.broadcasted_iota(jnp.int32, weights.shape, 0)
        factor = jnp.sum(jnp.where(row == prompt, weights, 0.0), axis=0, keepdims=True)
        value = dec_ref[...].astype(jnp.float32) * factor
        live = src_live[prompt, column] > 0
        out_ref[0] = jnp.where(live, value, 0.0).astype(out_ref.dtype)

    @pl.when(column >= ACTIVE_SLOTS)
    def _():
        live = tgt_live[prompt, column - ACTIVE_SLOTS] > 0
        out_ref[0] = jnp.where(live, enc_ref[...], jnp.zeros_like(enc_ref[...]))


def select_blocks(decoder, encoder, activation, src_loc, tgt_loc, src_live, tgt_live):
    rows, _ = decoder.shape
    prompts = activation.shape[0]
    slots = ACTIVE_SLOTS

    def dec_map(p, j, sl, tl, sv, tv):
        return (0, sl[p, jnp.minimum(j, slots - 1)])

    def enc_map(p, j, sl, tl, sv, tv):
        return (0, tl[p, jnp.maximum(j - slots, 0)])

    def out_map(p, j, sl, tl, sv, tv):
        return (p, 0, j)

    grid_spec = pltpu.PrefetchScalarGridSpec(
        num_scalar_prefetch=4,
        grid=(prompts, 2 * slots),
        in_specs=[
            pl.BlockSpec((rows, BLK), dec_map),
            pl.BlockSpec((rows, BLK), enc_map),
            pl.BlockSpec((prompts, BLK), dec_map),
        ],
        out_specs=pl.BlockSpec((1, rows, BLK), out_map),
    )
    block_bytes = rows * BLK * 2
    return pl.pallas_call(
        select_kernel,
        grid_spec=grid_spec,
        out_shape=jax.ShapeDtypeStruct((prompts, rows, 2 * slots * BLK), jnp.bfloat16),
        cost_estimate=pl.CostEstimate(
            flops=prompts * slots * rows * BLK,
            transcendentals=0,
            bytes_accessed=4 * prompts * slots * block_bytes,
        ),
    )(src_loc, tgt_loc, src_live, tgt_live, decoder, encoder, activation)


def slot_tables(blocks, counts, layer, quarter, local_blocks):
    ids = lax.dynamic_index_in_dim(blocks, layer, 1, False)
    count = lax.dynamic_index_in_dim(counts, layer, 1, False)
    slot = jnp.arange(ids.shape[1], dtype=jnp.int32)[None, :]
    live = (slot < count[:, None]) & (ids // local_blocks == quarter)
    return (ids % local_blocks).astype(jnp.int32), live.astype(jnp.int32)


def on_device(decoder, encoder, activation, blocks, counts):
    group_count = lax.axis_size("lg")
    layer_group = lax.axis_index("lg")
    quarter = lax.axis_index("q")
    fblk = lax.axis_index("fblk")
    fblk_count = lax.axis_size("fblk")
    local_blocks = decoder.shape[1] // BLK
    active_width = ACTIVE_SLOTS * BLK
    share = active_width // fblk_count

    src_loc, src_live = slot_tables(blocks, counts, layer_group, quarter, local_blocks)
    tgt_loc, tgt_live = slot_tables(blocks, counts, layer_group + 1, quarter, local_blocks)
    combined = select_blocks(decoder, encoder, activation, src_loc, tgt_loc, src_live, tgt_live)
    combined = lax.psum_scatter(combined, "q", scatter_dimension=0, tiled=True)
    source = combined[0, :, :active_width]
    target = combined[0, :, active_width:]

    partial_gram = lax.dot_general(
        target, source, (((0,), (0,)), ((), ())), preferred_element_type=jnp.float32
    ).astype(jnp.bfloat16)
    gram_sum = lax.psum(partial_gram, "fblk").astype(jnp.float32)
    live_rows = (lax.dynamic_slice(counts, (quarter, layer_group), (1, 1))[0, 0] * BLK).astype(
        jnp.float32
    )
    row_mean = jnp.sum(jnp.abs(gram_sum), axis=1) / live_rows
    edges = (0.7 * gram_sum / ((row_mean[:, None] + 1e-06) * jnp.sqrt(live_rows))).astype(
        jnp.bfloat16
    )

    mine = lax.dynamic_slice_in_dim(edges, fblk * share, share, 1).T
    width = share // CHUNKS
    forward = [(index, index + 1) for index in range(group_count - 1)]
    for step in range(1, group_count + CHUNKS - 1):
        sent = jnp.clip(step - 1 - layer_group, 0, CHUNKS - 1)
        outgoing = lax.dynamic_slice_in_dim(mine, sent * width, width, 0)
        previous = lax.ppermute(outgoing, "lg", forward)
        product = lax.dot_general(
            previous, edges, (((1,), (1,)), ((), ())), preferred_element_type=jnp.float32
        ).astype(jnp.bfloat16)
        chunk = step - layer_group
        valid = (layer_group >= 1) & (chunk >= 0) & (chunk < CHUNKS)
        place = jnp.clip(chunk, 0, CHUNKS - 1)
        kept = lax.dynamic_slice_in_dim(mine, place * width, width, 0)
        mine = lax.dynamic_update_slice_in_dim(
            mine, jnp.where(valid, product, kept), place * width, 0
        )

    parts = []
    for shift in range(fblk_count):
        wanted = (fblk + shift) % fblk_count
        piece = lax.dynamic_slice_in_dim(mine, wanted * share, share, 1)
        if shift:
            pairs = [(index, (index + shift) % fblk_count) for index in range(fblk_count)]
            piece = lax.ppermute(piece, "fblk", pairs)
        parts.append(piece.T)
    ordered = [parts[(fblk_count - m) % fblk_count] for m in range(fblk_count)]
    doubled = jnp.concatenate(ordered + ordered, axis=1)
    rows = lax.dynamic_slice_in_dim(doubled, (fblk_count - fblk) * share, active_width, 1)
    influence = (jnp.sqrt(jnp.float32(active_width)) * rows.astype(jnp.float32)).astype(
        jnp.bfloat16
    )
    return influence[None]


def solution(mesh):
    layer_count = mesh.shape["layer"]
    fblk_count = mesh.shape["fblk"]
    split = Mesh(
        mesh.devices.reshape(LAYERS, layer_count // LAYERS, fblk_count), ("lg", "q", "fblk")
    )
    layer = ("lg", "q")
    in_specs = (P("fblk", layer), P("fblk", layer), P(None, layer), P(), P())
    out_specs = P(layer, "fblk", None)
    return jax.shard_map(
        on_device, mesh=split, in_specs=in_specs, out_specs=out_specs, check_vma=False
    )
```

```python
import jax
import jax.numpy as jnp
from jax import lax
from jax.experimental import pallas as pl
from jax.experimental.pallas import tpu as pltpu
from jax.sharding import Mesh
from jax.sharding import PartitionSpec as P

BLK = 512
ACTIVE_SLOTS = 3
LAYERS = 8
CHUNKS = 1
ROW_TILES = 3


def select_kernel(src_loc, tgt_loc, src_live, tgt_live, dec_ref, enc_ref, act_ref, out_ref):
    prompt = pl.program_id(0)
    column = pl.program_id(1)

    @pl.when(column < ACTIVE_SLOTS)
    def _():
        weights = act_ref[...].astype(jnp.float32)
        row = lax.broadcasted_iota(jnp.int32, weights.shape, 0)
        factor = jnp.sum(jnp.where(row == prompt, weights, 0.0), axis=0, keepdims=True)
        value = dec_ref[...].astype(jnp.float32) * factor
        live = src_live[prompt, column] > 0
        out_ref[0] = jnp.where(live, value, 0.0).astype(out_ref.dtype)

    @pl.when(column >= ACTIVE_SLOTS)
    def _():
        live = tgt_live[prompt, column - ACTIVE_SLOTS] > 0
        out_ref[0] = jnp.where(live, enc_ref[...], jnp.zeros_like(enc_ref[...]))


def select_blocks(decoder, encoder, activation, src_loc, tgt_loc, src_live, tgt_live):
    rows, _ = decoder.shape
    prompts = activation.shape[0]
    slots = ACTIVE_SLOTS

    tile = rows // ROW_TILES

    def dec_map(p, j, r, sl, tl, sv, tv):
        return (r, sl[p, jnp.minimum(j, slots - 1)])

    def enc_map(p, j, r, sl, tl, sv, tv):
        return (r, tl[p, jnp.maximum(j - slots, 0)])

    def act_map(p, j, r, sl, tl, sv, tv):
        return (0, sl[p, jnp.minimum(j, slots - 1)])

    def out_map(p, j, r, sl, tl, sv, tv):
        return (p, r, j)

    grid_spec = pltpu.PrefetchScalarGridSpec(
        num_scalar_prefetch=4,
        grid=(prompts, 2 * slots, ROW_TILES),
        in_specs=[
            pl.BlockSpec((tile, BLK), dec_map),
            pl.BlockSpec((tile, BLK), enc_map),
            pl.BlockSpec((prompts, BLK), act_map),
        ],
        out_specs=pl.BlockSpec((1, tile, BLK), out_map),
    )
    block_bytes = rows * BLK * 2
    return pl.pallas_call(
        select_kernel,
        grid_spec=grid_spec,
        out_shape=jax.ShapeDtypeStruct((prompts, rows, 2 * slots * BLK), jnp.bfloat16),
        cost_estimate=pl.CostEstimate(
            flops=prompts * slots * rows * BLK,
            transcendentals=0,
            bytes_accessed=4 * prompts * slots * block_bytes,
        ),
    )(src_loc, tgt_loc, src_live, tgt_live, decoder, encoder, activation)


def slot_tables(blocks, counts, layer, quarter, local_blocks):
    ids = lax.dynamic_index_in_dim(blocks, layer, 1, False)
    count = lax.dynamic_index_in_dim(counts, layer, 1, False)
    slot = jnp.arange(ids.shape[1], dtype=jnp.int32)[None, :]
    live = (slot < count[:, None]) & (ids // local_blocks == quarter)
    return (ids % local_blocks).astype(jnp.int32), live.astype(jnp.int32)


def on_device(decoder, encoder, activation, blocks, counts):
    group_count = lax.axis_size("lg")
    layer_group = lax.axis_index("lg")
    quarter = lax.axis_index("q")
    fblk = lax.axis_index("fblk")
    fblk_count = lax.axis_size("fblk")
    local_blocks = decoder.shape[1] // BLK
    active_width = ACTIVE_SLOTS * BLK
    share = active_width // fblk_count

    src_loc, src_live = slot_tables(blocks, counts, layer_group, quarter, local_blocks)
    tgt_loc, tgt_live = slot_tables(blocks, counts, layer_group + 1, quarter, local_blocks)
    combined = select_blocks(decoder, encoder, activation, src_loc, tgt_loc, src_live, tgt_live)
    combined = lax.psum_scatter(combined, "q", scatter_dimension=0, tiled=True)
    source = combined[0, :, :active_width]
    target = combined[0, :, active_width:]

    partial_gram = lax.dot_general(
        target, source, (((0,), (0,)), ((), ())), preferred_element_type=jnp.float32
    ).astype(jnp.bfloat16)
    gram_sum = lax.psum(partial_gram, "fblk").astype(jnp.float32)
    live_rows = (lax.dynamic_slice(counts, (quarter, layer_group), (1, 1))[0, 0] * BLK).astype(
        jnp.float32
    )
    row_mean = jnp.sum(jnp.abs(gram_sum), axis=1) / live_rows
    edges = (0.7 * gram_sum / ((row_mean[:, None] + 1e-06) * jnp.sqrt(live_rows))).astype(
        jnp.bfloat16
    )

    mine = lax.dynamic_slice_in_dim(edges, fblk * share, share, 1).T
    width = share // CHUNKS
    forward = [(index, index + 1) for index in range(group_count - 1)]
    for step in range(1, group_count + CHUNKS - 1):
        sent = jnp.clip(step - 1 - layer_group, 0, CHUNKS - 1)
        outgoing = lax.dynamic_slice_in_dim(mine, sent * width, width, 0)
        previous = lax.ppermute(outgoing, "lg", forward)
        product = lax.dot_general(
            previous, edges, (((1,), (1,)), ((), ())), preferred_element_type=jnp.float32
        ).astype(jnp.bfloat16)
        chunk = step - layer_group
        valid = (layer_group >= 1) & (chunk >= 0) & (chunk < CHUNKS)
        place = jnp.clip(chunk, 0, CHUNKS - 1)
        kept = lax.dynamic_slice_in_dim(mine, place * width, width, 0)
        mine = lax.dynamic_update_slice_in_dim(
            mine, jnp.where(valid, product, kept), place * width, 0
        )

    parts = []
    for shift in range(fblk_count):
        wanted = (fblk + shift) % fblk_count
        piece = lax.dynamic_slice_in_dim(mine, wanted * share, share, 1)
        if shift:
            pairs = [(index, (index + shift) % fblk_count) for index in range(fblk_count)]
            piece = lax.ppermute(piece, "fblk", pairs)
        parts.append(piece.T)
    ordered = [parts[(fblk_count - m) % fblk_count] for m in range(fblk_count)]
    doubled = jnp.concatenate(ordered + ordered, axis=1)
    rows = lax.dynamic_slice_in_dim(doubled, (fblk_count - fblk) * share, active_width, 1)
    influence = (jnp.sqrt(jnp.float32(active_width)) * rows.astype(jnp.float32)).astype(
        jnp.bfloat16
    )
    return influence[None]


def solution(mesh):
    layer_count = mesh.shape["layer"]
    fblk_count = mesh.shape["fblk"]
    split = Mesh(
        mesh.devices.reshape(LAYERS, layer_count // LAYERS, fblk_count), ("lg", "q", "fblk")
    )
    layer = ("lg", "q")
    in_specs = (P("fblk", layer), P("fblk", layer), P(None, layer), P(), P())
    out_specs = P(layer, "fblk", None)
    return jax.shard_map(
        on_device, mesh=split, in_specs=in_specs, out_specs=out_specs, check_vma=False
    )
```

```python
import jax
import jax.numpy as jnp
from jax import lax
from jax.experimental import pallas as pl
from jax.experimental.pallas import tpu as pltpu
from jax.sharding import Mesh
from jax.sharding import PartitionSpec as P

BLK = 512
ACTIVE_SLOTS = 3
LAYERS = 8
CHUNKS = 1
ROW_TILE = 64


def select_kernel(src_loc, tgt_loc, src_live, tgt_live, dec_ref, enc_ref, act_ref, out_ref):
    prompt = pl.program_id(0)
    column = pl.program_id(1)
    rows = dec_ref.shape[0]
    steps = rows // ROW_TILE

    @pl.when(column < ACTIVE_SLOTS)
    def _():
        weights = act_ref[...].astype(jnp.float32)
        row = lax.broadcasted_iota(jnp.int32, weights.shape, 0)
        factor = jnp.sum(jnp.where(row == prompt, weights, 0.0), axis=0, keepdims=True)
        live = src_live[prompt, column] > 0

        def body(index, carry):
            lower = pl.multiple_of(index * ROW_TILE, ROW_TILE)
            value = dec_ref[pl.ds(lower, ROW_TILE), :].astype(jnp.float32) * factor
            out_ref[0, pl.ds(lower, ROW_TILE), :] = jnp.where(live, value, 0.0).astype(
                out_ref.dtype
            )
            return carry

        lax.fori_loop(0, steps, body, 0)

    @pl.when(column >= ACTIVE_SLOTS)
    def _():
        live = tgt_live[prompt, column - ACTIVE_SLOTS] > 0

        def body(index, carry):
            lower = pl.multiple_of(index * ROW_TILE, ROW_TILE)
            value = enc_ref[pl.ds(lower, ROW_TILE), :]
            out_ref[0, pl.ds(lower, ROW_TILE), :] = jnp.where(live, value, jnp.zeros_like(value))
            return carry

        lax.fori_loop(0, steps, body, 0)


def select_blocks(decoder, encoder, activation, src_loc, tgt_loc, src_live, tgt_live):
    rows, _ = decoder.shape
    prompts = activation.shape[0]
    slots = ACTIVE_SLOTS

    def dec_map(p, j, sl, tl, sv, tv):
        return (0, sl[p, jnp.minimum(j, slots - 1)])

    def enc_map(p, j, sl, tl, sv, tv):
        return (0, tl[p, jnp.maximum(j - slots, 0)])

    def out_map(p, j, sl, tl, sv, tv):
        return (p, 0, j)

    grid_spec = pltpu.PrefetchScalarGridSpec(
        num_scalar_prefetch=4,
        grid=(prompts, 2 * slots),
        in_specs=[
            pl.BlockSpec((rows, BLK), dec_map),
            pl.BlockSpec((rows, BLK), enc_map),
            pl.BlockSpec((prompts, BLK), dec_map),
        ],
        out_specs=pl.BlockSpec((1, rows, BLK), out_map),
    )
    block_bytes = rows * BLK * 2
    return pl.pallas_call(
        select_kernel,
        grid_spec=grid_spec,
        out_shape=jax.ShapeDtypeStruct((prompts, rows, 2 * slots * BLK), jnp.bfloat16),
        cost_estimate=pl.CostEstimate(
            flops=prompts * slots * rows * BLK,
            transcendentals=0,
            bytes_accessed=4 * prompts * slots * block_bytes,
        ),
    )(src_loc, tgt_loc, src_live, tgt_live, decoder, encoder, activation)


def slot_tables(blocks, counts, layer, quarter, local_blocks):
    ids = lax.dynamic_index_in_dim(blocks, layer, 1, False)
    count = lax.dynamic_index_in_dim(counts, layer, 1, False)
    slot = jnp.arange(ids.shape[1], dtype=jnp.int32)[None, :]
    live = (slot < count[:, None]) & (ids // local_blocks == quarter)
    return (ids % local_blocks).astype(jnp.int32), live.astype(jnp.int32)


def on_device(decoder, encoder, activation, blocks, counts):
    group_count = lax.axis_size("lg")
    layer_group = lax.axis_index("lg")
    quarter = lax.axis_index("q")
    fblk = lax.axis_index("fblk")
    fblk_count = lax.axis_size("fblk")
    local_blocks = decoder.shape[1] // BLK
    active_width = ACTIVE_SLOTS * BLK
    share = active_width // fblk_count

    src_loc, src_live = slot_tables(blocks, counts, layer_group, quarter, local_blocks)
    tgt_loc, tgt_live = slot_tables(blocks, counts, layer_group + 1, quarter, local_blocks)
    combined = select_blocks(decoder, encoder, activation, src_loc, tgt_loc, src_live, tgt_live)
    combined = lax.psum_scatter(combined, "q", scatter_dimension=0, tiled=True)
    source = combined[0, :, :active_width]
    target = combined[0, :, active_width:]

    partial_gram = lax.dot_general(
        target, source, (((0,), (0,)), ((), ())), preferred_element_type=jnp.float32
    ).astype(jnp.bfloat16)
    gram_sum = lax.psum(partial_gram, "fblk").astype(jnp.float32)
    live_rows = (lax.dynamic_slice(counts, (quarter, layer_group), (1, 1))[0, 0] * BLK).astype(
        jnp.float32
    )
    row_mean = jnp.sum(jnp.abs(gram_sum), axis=1) / live_rows
    edges = (0.7 * gram_sum / ((row_mean[:, None] + 1e-06) * jnp.sqrt(live_rows))).astype(
        jnp.bfloat16
    )

    edges_t = edges.T
    mine = lax.dynamic_slice_in_dim(edges_t, fblk * share, share, 0)
    width = share // CHUNKS
    forward = [(index, index + 1) for index in range(group_count - 1)]
    for step in range(1, group_count + CHUNKS - 1):
        sent = jnp.clip(step - 1 - layer_group, 0, CHUNKS - 1)
        outgoing = lax.dynamic_slice_in_dim(mine, sent * width, width, 0)
        previous = lax.ppermute(outgoing, "lg", forward)
        product = jnp.dot(previous, edges_t, preferred_element_type=jnp.float32).astype(
            jnp.bfloat16
        )
        chunk = step - layer_group
        valid = (layer_group >= 1) & (chunk >= 0) & (chunk < CHUNKS)
        place = jnp.clip(chunk, 0, CHUNKS - 1)
        kept = lax.dynamic_slice_in_dim(mine, place * width, width, 0)
        mine = lax.dynamic_update_slice_in_dim(
            mine, jnp.where(valid, product, kept), place * width, 0
        )

    parts = []
    for shift in range(fblk_count):
        wanted = (fblk + shift) % fblk_count
        piece = lax.dynamic_slice_in_dim(mine, wanted * share, share, 1)
        if shift:
            pairs = [(index, (index + shift) % fblk_count) for index in range(fblk_count)]
            piece = lax.ppermute(piece, "fblk", pairs)
        parts.append(piece.T)
    ordered = [parts[(fblk_count - m) % fblk_count] for m in range(fblk_count)]
    doubled = jnp.concatenate(ordered + ordered, axis=1)
    rows = lax.dynamic_slice_in_dim(doubled, (fblk_count - fblk) * share, active_width, 1)
    influence = (jnp.sqrt(jnp.float32(active_width)) * rows.astype(jnp.float32)).astype(
        jnp.bfloat16
    )
    return influence[None]


def solution(mesh):
    layer_count = mesh.shape["layer"]
    fblk_count = mesh.shape["fblk"]
    split = Mesh(
        mesh.devices.reshape(LAYERS, layer_count // LAYERS, fblk_count), ("lg", "q", "fblk")
    )
    layer = ("lg", "q")
    in_specs = (P("fblk", layer), P("fblk", layer), P(None, layer), P(), P())
    out_specs = P(layer, "fblk", None)
    return jax.shard_map(
        on_device, mesh=split, in_specs=in_specs, out_specs=out_specs, check_vma=False
    )
```

```python
import functools

import jax
import jax.numpy as jnp
from jax import lax
from jax.experimental import pallas as pl
from jax.experimental.pallas import tpu as pltpu
from jax.sharding import Mesh
from jax.sharding import PartitionSpec as P

BLK = 512
ACTIVE_SLOTS = 3
LAYERS = 8
CHUNKS = 1
ROW_TILE = 64


def select_kernel(block_loc, block_live, matrix_ref, act_ref, out_ref, scaled):
    prompt = pl.program_id(0)
    slot = pl.program_id(1)
    rows = matrix_ref.shape[0]
    steps = rows // ROW_TILE
    live = block_live[prompt, slot] > 0
    if scaled:
        weights = act_ref[...].astype(jnp.float32)
        row = lax.broadcasted_iota(jnp.int32, weights.shape, 0)
        factor = jnp.sum(jnp.where(row == prompt, weights, 0.0), axis=0, keepdims=True)

    def body(index, carry):
        lower = pl.multiple_of(index * ROW_TILE, ROW_TILE)
        value = matrix_ref[pl.ds(lower, ROW_TILE), :]
        if scaled:
            value = jnp.where(live, value.astype(jnp.float32) * factor, 0.0)
        else:
            value = jnp.where(live, value, jnp.zeros_like(value))
        out_ref[0, pl.ds(lower, ROW_TILE), :] = value.astype(out_ref.dtype)
        return carry

    lax.fori_loop(0, steps, body, 0)


def select_blocks(matrix, activation, block_loc, block_live, scaled):
    rows, _ = matrix.shape
    prompts = activation.shape[0]
    slots = ACTIVE_SLOTS

    def in_map(p, j, loc, live):
        return (0, loc[p, j])

    def out_map(p, j, loc, live):
        return (p, 0, j)

    grid_spec = pltpu.PrefetchScalarGridSpec(
        num_scalar_prefetch=2,
        grid=(prompts, slots),
        in_specs=[
            pl.BlockSpec((rows, BLK), in_map),
            pl.BlockSpec((prompts, BLK), in_map),
        ],
        out_specs=pl.BlockSpec((1, rows, BLK), out_map),
    )
    block_bytes = rows * BLK * 2
    return pl.pallas_call(
        functools.partial(select_kernel, scaled=scaled),
        grid_spec=grid_spec,
        out_shape=jax.ShapeDtypeStruct((prompts, rows, slots * BLK), jnp.bfloat16),
        cost_estimate=pl.CostEstimate(
            flops=prompts * slots * rows * BLK,
            transcendentals=0,
            bytes_accessed=2 * prompts * slots * block_bytes,
        ),
    )(block_loc, block_live, matrix, activation)


def slot_tables(blocks, counts, layer, quarter, local_blocks):
    ids = lax.dynamic_index_in_dim(blocks, layer, 1, False)
    count = lax.dynamic_index_in_dim(counts, layer, 1, False)
    slot = jnp.arange(ids.shape[1], dtype=jnp.int32)[None, :]
    live = (slot < count[:, None]) & (ids // local_blocks == quarter)
    return (ids % local_blocks).astype(jnp.int32), live.astype(jnp.int32)


def on_device(decoder, encoder, activation, blocks, counts):
    group_count = lax.axis_size("lg")
    layer_group = lax.axis_index("lg")
    quarter = lax.axis_index("q")
    fblk = lax.axis_index("fblk")
    fblk_count = lax.axis_size("fblk")
    local_blocks = decoder.shape[1] // BLK
    active_width = ACTIVE_SLOTS * BLK
    share = active_width // fblk_count

    src_loc, src_live = slot_tables(blocks, counts, layer_group, quarter, local_blocks)
    tgt_loc, tgt_live = slot_tables(blocks, counts, layer_group + 1, quarter, local_blocks)
    source = select_blocks(decoder, activation, src_loc, src_live, True)
    source = lax.psum_scatter(source, "q", scatter_dimension=0, tiled=True)[0]
    target = select_blocks(encoder, activation, tgt_loc, tgt_live, False)
    target = lax.psum_scatter(target, "q", scatter_dimension=0, tiled=True)[0]

    partial_gram = lax.dot_general(
        target, source, (((0,), (0,)), ((), ())), preferred_element_type=jnp.float32
    ).astype(jnp.bfloat16)
    gram_sum = lax.psum(partial_gram, "fblk").astype(jnp.float32)
    live_rows = (lax.dynamic_slice(counts, (quarter, layer_group), (1, 1))[0, 0] * BLK).astype(
        jnp.float32
    )
    row_mean = jnp.sum(jnp.abs(gram_sum), axis=1) / live_rows
    edges = (0.7 * gram_sum / ((row_mean[:, None] + 1e-06) * jnp.sqrt(live_rows))).astype(
        jnp.bfloat16
    )

    edges_t = edges.T
    mine = lax.dynamic_slice_in_dim(edges_t, fblk * share, share, 0)
    width = share // CHUNKS
    forward = [(index, index + 1) for index in range(group_count - 1)]
    for step in range(1, group_count + CHUNKS - 1):
        sent = jnp.clip(step - 1 - layer_group, 0, CHUNKS - 1)
        outgoing = lax.dynamic_slice_in_dim(mine, sent * width, width, 0)
        previous = lax.ppermute(outgoing, "lg", forward)
        product = jnp.dot(previous, edges_t, preferred_element_type=jnp.float32).astype(
            jnp.bfloat16
        )
        chunk = step - layer_group
        valid = (layer_group >= 1) & (chunk >= 0) & (chunk < CHUNKS)
        place = jnp.clip(chunk, 0, CHUNKS - 1)
        kept = lax.dynamic_slice_in_dim(mine, place * width, width, 0)
        mine = lax.dynamic_update_slice_in_dim(
            mine, jnp.where(valid, product, kept), place * width, 0
        )

    parts = []
    for shift in range(fblk_count):
        wanted = (fblk + shift) % fblk_count
        piece = lax.dynamic_slice_in_dim(mine, wanted * share, share, 1)
        if shift:
            pairs = [(index, (index + shift) % fblk_count) for index in range(fblk_count)]
            piece = lax.ppermute(piece, "fblk", pairs)
        parts.append(piece.T)
    ordered = [parts[(fblk_count - m) % fblk_count] for m in range(fblk_count)]
    doubled = jnp.concatenate(ordered + ordered, axis=1)
    rows = lax.dynamic_slice_in_dim(doubled, (fblk_count - fblk) * share, active_width, 1)
    influence = (jnp.sqrt(jnp.float32(active_width)) * rows.astype(jnp.float32)).astype(
        jnp.bfloat16
    )
    return influence[None]


def solution(mesh):
    layer_count = mesh.shape["layer"]
    fblk_count = mesh.shape["fblk"]
    split = Mesh(
        mesh.devices.reshape(LAYERS, layer_count // LAYERS, fblk_count), ("lg", "q", "fblk")
    )
    layer = ("lg", "q")
    in_specs = (P("fblk", layer), P("fblk", layer), P(None, layer), P(), P())
    out_specs = P(layer, "fblk", None)
    return jax.shard_map(
        on_device, mesh=split, in_specs=in_specs, out_specs=out_specs, check_vma=False
    )
```

```python
import jax
import jax.numpy as jnp
from jax import lax
from jax.experimental import pallas as pl
from jax.experimental.pallas import tpu as pltpu
from jax.sharding import Mesh
from jax.sharding import PartitionSpec as P

BLK = 512
ACTIVE_SLOTS = 3
LAYERS = 8
CHUNKS = 1
ROW_TILE = 64


def select_kernel(src_loc, tgt_loc, src_live, tgt_live, dec_ref, enc_ref, act_ref, out_ref):
    prompt = pl.program_id(0)
    column = pl.program_id(1)
    rows = dec_ref.shape[0]
    steps = rows // ROW_TILE

    @pl.when(column < ACTIVE_SLOTS)
    def _():
        weights = act_ref[...].astype(jnp.float32)
        row = lax.broadcasted_iota(jnp.int32, weights.shape, 0)
        factor = jnp.sum(jnp.where(row == prompt, weights, 0.0), axis=0, keepdims=True)
        live = src_live[prompt, column] > 0

        def body(index, carry):
            lower = pl.multiple_of(index * ROW_TILE, ROW_TILE)
            value = dec_ref[pl.ds(lower, ROW_TILE), :].astype(jnp.float32) * factor
            out_ref[0, pl.ds(lower, ROW_TILE), :] = jnp.where(live, value, 0.0).astype(
                out_ref.dtype
            )
            return carry

        lax.fori_loop(0, steps, body, 0)

    @pl.when(column >= ACTIVE_SLOTS)
    def _():
        live = tgt_live[prompt, column - ACTIVE_SLOTS] > 0

        def body(index, carry):
            lower = pl.multiple_of(index * ROW_TILE, ROW_TILE)
            value = enc_ref[pl.ds(lower, ROW_TILE), :]
            out_ref[0, pl.ds(lower, ROW_TILE), :] = jnp.where(live, value, jnp.zeros_like(value))
            return carry

        lax.fori_loop(0, steps, body, 0)


def select_blocks(decoder, encoder, activation, src_loc, tgt_loc, src_live, tgt_live):
    rows, _ = decoder.shape
    prompts = activation.shape[0]
    slots = ACTIVE_SLOTS

    def dec_map(p, j, sl, tl, sv, tv):
        return (0, sl[p, j])

    def enc_map(p, j, sl, tl, sv, tv):
        return (0, tl[p, j])

    def out_map(p, j, sl, tl, sv, tv):
        return (p, 0, j)

    grid_spec = pltpu.PrefetchScalarGridSpec(
        num_scalar_prefetch=4,
        grid=(prompts, 2 * slots),
        in_specs=[
            pl.BlockSpec((rows, BLK), dec_map),
            pl.BlockSpec((rows, BLK), enc_map),
            pl.BlockSpec((prompts, BLK), dec_map),
        ],
        out_specs=pl.BlockSpec((1, rows, BLK), out_map),
    )
    block_bytes = rows * BLK * 2
    return pl.pallas_call(
        select_kernel,
        grid_spec=grid_spec,
        out_shape=jax.ShapeDtypeStruct((prompts, rows, 2 * slots * BLK), jnp.bfloat16),
        cost_estimate=pl.CostEstimate(
            flops=prompts * slots * rows * BLK,
            transcendentals=0,
            bytes_accessed=4 * prompts * slots * block_bytes,
        ),
    )(src_loc, tgt_loc, src_live, tgt_live, decoder, encoder, activation)


def held_blocks(block_loc, block_live, first):
    prompts, slots = block_loc.shape
    column = jnp.arange(2 * slots)[None, :]
    index = jnp.clip(column - first, 0, slots - 1)
    value = jnp.take_along_axis(block_loc, jnp.broadcast_to(index, (prompts, 2 * slots)), axis=1)
    need = jnp.take_along_axis(block_live, jnp.broadcast_to(index, (prompts, 2 * slots)), axis=1) > 0
    need = need & (column >= first) & (column < first + slots)
    value = value.reshape(-1)
    need = need.reshape(-1)
    position = jnp.arange(value.shape[0])
    last = lax.cummax(jnp.where(need, position, -1), axis=0)
    earliest = jnp.argmax(need)
    last = jnp.where(last < 0, earliest, last)
    return jnp.take(value, last).reshape(prompts, 2 * slots).astype(jnp.int32)


def slot_tables(blocks, counts, layer, quarter, local_blocks):
    ids = lax.dynamic_index_in_dim(blocks, layer, 1, False)
    count = lax.dynamic_index_in_dim(counts, layer, 1, False)
    slot = jnp.arange(ids.shape[1], dtype=jnp.int32)[None, :]
    live = (slot < count[:, None]) & (ids // local_blocks == quarter)
    return (ids % local_blocks).astype(jnp.int32), live.astype(jnp.int32)


def on_device(decoder, encoder, activation, blocks, counts):
    group_count = lax.axis_size("lg")
    layer_group = lax.axis_index("lg")
    quarter = lax.axis_index("q")
    fblk = lax.axis_index("fblk")
    fblk_count = lax.axis_size("fblk")
    local_blocks = decoder.shape[1] // BLK
    active_width = ACTIVE_SLOTS * BLK
    share = active_width // fblk_count

    src_loc, src_live = slot_tables(blocks, counts, layer_group, quarter, local_blocks)
    tgt_loc, tgt_live = slot_tables(blocks, counts, layer_group + 1, quarter, local_blocks)
    dec_held = held_blocks(src_loc, src_live, 0)
    enc_held = held_blocks(tgt_loc, tgt_live, ACTIVE_SLOTS)
    combined = select_blocks(decoder, encoder, activation, dec_held, enc_held, src_live, tgt_live)
    combined = lax.psum_scatter(combined, "q", scatter_dimension=0, tiled=True)
    source = combined[0, :, :active_width]
    target = combined[0, :, active_width:]

    partial_gram = lax.dot_general(
        target, source, (((0,), (0,)), ((), ())), preferred_element_type=jnp.float32
    ).astype(jnp.bfloat16)
    gram_sum = lax.psum(partial_gram, "fblk").astype(jnp.float32)
    live_rows = (lax.dynamic_slice(counts, (quarter, layer_group), (1, 1))[0, 0] * BLK).astype(
        jnp.float32
    )
    row_mean = jnp.sum(jnp.abs(gram_sum), axis=1) / live_rows
    edges = (0.7 * gram_sum / ((row_mean[:, None] + 1e-06) * jnp.sqrt(live_rows))).astype(
        jnp.bfloat16
    )

    edges_t = edges.T
    mine = lax.dynamic_slice_in_dim(edges_t, fblk * share, share, 0)
    width = share // CHUNKS
    forward = [(index, index + 1) for index in range(group_count - 1)]
    for step in range(1, group_count + CHUNKS - 1):
        sent = jnp.clip(step - 1 - layer_group, 0, CHUNKS - 1)
        outgoing = lax.dynamic_slice_in_dim(mine, sent * width, width, 0)
        previous = lax.ppermute(outgoing, "lg", forward)
        product = jnp.dot(previous, edges_t, preferred_element_type=jnp.float32).astype(
            jnp.bfloat16
        )
        chunk = step - layer_group
        valid = (layer_group >= 1) & (chunk >= 0) & (chunk < CHUNKS)
        place = jnp.clip(chunk, 0, CHUNKS - 1)
        kept = lax.dynamic_slice_in_dim(mine, place * width, width, 0)
        mine = lax.dynamic_update_slice_in_dim(
            mine, jnp.where(valid, product, kept), place * width, 0
        )

    parts = []
    for shift in range(fblk_count):
        wanted = (fblk + shift) % fblk_count
        piece = lax.dynamic_slice_in_dim(mine, wanted * share, share, 1)
        if shift:
            pairs = [(index, (index + shift) % fblk_count) for index in range(fblk_count)]
            piece = lax.ppermute(piece, "fblk", pairs)
        parts.append(piece.T)
    ordered = [parts[(fblk_count - m) % fblk_count] for m in range(fblk_count)]
    doubled = jnp.concatenate(ordered + ordered, axis=1)
    rows = lax.dynamic_slice_in_dim(doubled, (fblk_count - fblk) * share, active_width, 1)
    influence = (jnp.sqrt(jnp.float32(active_width)) * rows.astype(jnp.float32)).astype(
        jnp.bfloat16
    )
    return influence[None]


def solution(mesh):
    layer_count = mesh.shape["layer"]
    fblk_count = mesh.shape["fblk"]
    split = Mesh(
        mesh.devices.reshape(LAYERS, layer_count // LAYERS, fblk_count), ("lg", "q", "fblk")
    )
    layer = ("lg", "q")
    in_specs = (P("fblk", layer), P("fblk", layer), P(None, layer), P(), P())
    out_specs = P(layer, "fblk", None)
    return jax.shard_map(
        on_device, mesh=split, in_specs=in_specs, out_specs=out_specs, check_vma=False
    )
```

```python
import jax
import jax.numpy as jnp
from jax import lax
from jax.experimental import pallas as pl
from jax.experimental.pallas import tpu as pltpu
from jax.sharding import Mesh
from jax.sharding import PartitionSpec as P

BLK = 512
ACTIVE_SLOTS = 3
LAYERS = 8
CHUNKS = 1
ROW_TILE = 64


def select_kernel(src_loc, tgt_loc, src_live, tgt_live, *refs):
    dec_refs = refs[:ACTIVE_SLOTS]
    enc_refs = refs[ACTIVE_SLOTS : 2 * ACTIVE_SLOTS]
    act_refs = refs[2 * ACTIVE_SLOTS : 3 * ACTIVE_SLOTS]
    out_ref = refs[3 * ACTIVE_SLOTS]
    prompt = pl.program_id(0)
    kind = pl.program_id(1)
    rows = dec_refs[0].shape[0]
    steps = rows // ROW_TILE

    @pl.when(kind == 0)
    def _():
        for slot in range(ACTIVE_SLOTS):
            weights = act_refs[slot][...].astype(jnp.float32)
            row = lax.broadcasted_iota(jnp.int32, weights.shape, 0)
            factor = jnp.sum(jnp.where(row == prompt, weights, 0.0), axis=0, keepdims=True)
            live = src_live[prompt, slot] > 0
            matrix_ref = dec_refs[slot]

            def body(index, carry, matrix_ref=matrix_ref, factor=factor, live=live, slot=slot):
                lower = pl.multiple_of(index * ROW_TILE, ROW_TILE)
                value = matrix_ref[pl.ds(lower, ROW_TILE), :].astype(jnp.float32) * factor
                out_ref[0, pl.ds(lower, ROW_TILE), pl.ds(slot * BLK, BLK)] = jnp.where(
                    live, value, 0.0
                ).astype(out_ref.dtype)
                return carry

            lax.fori_loop(0, steps, body, 0)

    @pl.when(kind == 1)
    def _():
        for slot in range(ACTIVE_SLOTS):
            live = tgt_live[prompt, slot] > 0
            matrix_ref = enc_refs[slot]

            def body(index, carry, matrix_ref=matrix_ref, live=live, slot=slot):
                lower = pl.multiple_of(index * ROW_TILE, ROW_TILE)
                value = matrix_ref[pl.ds(lower, ROW_TILE), :]
                out_ref[0, pl.ds(lower, ROW_TILE), pl.ds(slot * BLK, BLK)] = jnp.where(
                    live, value, jnp.zeros_like(value)
                )
                return carry

            lax.fori_loop(0, steps, body, 0)


def select_blocks(decoder, encoder, activation, src_loc, tgt_loc, src_live, tgt_live):
    rows, _ = decoder.shape
    prompts = activation.shape[0]
    slots = ACTIVE_SLOTS

    def dec_map(slot):
        return lambda p, k, sl, tl, sv, tv: (0, sl[p, slot])

    def enc_map(slot):
        return lambda p, k, sl, tl, sv, tv: (0, tl[p, slot])

    def out_map(p, k, sl, tl, sv, tv):
        return (p, 0, k)

    grid_spec = pltpu.PrefetchScalarGridSpec(
        num_scalar_prefetch=4,
        grid=(prompts, 2),
        in_specs=[pl.BlockSpec((rows, BLK), dec_map(slot)) for slot in range(slots)]
        + [pl.BlockSpec((rows, BLK), enc_map(slot)) for slot in range(slots)]
        + [pl.BlockSpec((prompts, BLK), dec_map(slot)) for slot in range(slots)],
        out_specs=pl.BlockSpec((1, rows, slots * BLK), out_map),
    )
    block_bytes = rows * BLK * 2
    return pl.pallas_call(
        select_kernel,
        grid_spec=grid_spec,
        out_shape=jax.ShapeDtypeStruct((prompts, rows, 2 * slots * BLK), jnp.bfloat16),
        cost_estimate=pl.CostEstimate(
            flops=prompts * slots * rows * BLK,
            transcendentals=0,
            bytes_accessed=4 * prompts * slots * block_bytes,
        ),
    )(
        src_loc,
        tgt_loc,
        src_live,
        tgt_live,
        *([decoder] * slots),
        *([encoder] * slots),
        *([activation] * slots),
    )


def slot_tables(blocks, counts, layer, quarter, local_blocks):
    ids = lax.dynamic_index_in_dim(blocks, layer, 1, False)
    count = lax.dynamic_index_in_dim(counts, layer, 1, False)
    slot = jnp.arange(ids.shape[1], dtype=jnp.int32)[None, :]
    live = (slot < count[:, None]) & (ids // local_blocks == quarter)
    return (ids % local_blocks).astype(jnp.int32), live.astype(jnp.int32)


def on_device(decoder, encoder, activation, blocks, counts):
    group_count = lax.axis_size("lg")
    layer_group = lax.axis_index("lg")
    quarter = lax.axis_index("q")
    fblk = lax.axis_index("fblk")
    fblk_count = lax.axis_size("fblk")
    local_blocks = decoder.shape[1] // BLK
    active_width = ACTIVE_SLOTS * BLK
    share = active_width // fblk_count

    src_loc, src_live = slot_tables(blocks, counts, layer_group, quarter, local_blocks)
    tgt_loc, tgt_live = slot_tables(blocks, counts, layer_group + 1, quarter, local_blocks)
    combined = select_blocks(decoder, encoder, activation, src_loc, tgt_loc, src_live, tgt_live)
    combined = lax.psum_scatter(combined, "q", scatter_dimension=0, tiled=True)
    source = combined[0, :, :active_width]
    target = combined[0, :, active_width:]

    partial_gram = lax.dot_general(
        target, source, (((0,), (0,)), ((), ())), preferred_element_type=jnp.float32
    ).astype(jnp.bfloat16)
    gram_sum = lax.psum(partial_gram, "fblk").astype(jnp.float32)
    live_rows = (lax.dynamic_slice(counts, (quarter, layer_group), (1, 1))[0, 0] * BLK).astype(
        jnp.float32
    )
    row_mean = jnp.sum(jnp.abs(gram_sum), axis=1) / live_rows
    edges = (0.7 * gram_sum / ((row_mean[:, None] + 1e-06) * jnp.sqrt(live_rows))).astype(
        jnp.bfloat16
    )

    edges_t = edges.T
    mine = lax.dynamic_slice_in_dim(edges_t, fblk * share, share, 0)
    width = share // CHUNKS
    forward = [(index, index + 1) for index in range(group_count - 1)]
    for step in range(1, group_count + CHUNKS - 1):
        sent = jnp.clip(step - 1 - layer_group, 0, CHUNKS - 1)
        outgoing = lax.dynamic_slice_in_dim(mine, sent * width, width, 0)
        previous = lax.ppermute(outgoing, "lg", forward)
        product = jnp.dot(previous, edges_t, preferred_element_type=jnp.float32).astype(
            jnp.bfloat16
        )
        chunk = step - layer_group
        valid = (layer_group >= 1) & (chunk >= 0) & (chunk < CHUNKS)
        place = jnp.clip(chunk, 0, CHUNKS - 1)
        kept = lax.dynamic_slice_in_dim(mine, place * width, width, 0)
        mine = lax.dynamic_update_slice_in_dim(
            mine, jnp.where(valid, product, kept), place * width, 0
        )

    parts = []
    for shift in range(fblk_count):
        wanted = (fblk + shift) % fblk_count
        piece = lax.dynamic_slice_in_dim(mine, wanted * share, share, 1)
        if shift:
            pairs = [(index, (index + shift) % fblk_count) for index in range(fblk_count)]
            piece = lax.ppermute(piece, "fblk", pairs)
        parts.append(piece.T)
    ordered = [parts[(fblk_count - m) % fblk_count] for m in range(fblk_count)]
    doubled = jnp.concatenate(ordered + ordered, axis=1)
    rows = lax.dynamic_slice_in_dim(doubled, (fblk_count - fblk) * share, active_width, 1)
    influence = (jnp.sqrt(jnp.float32(active_width)) * rows.astype(jnp.float32)).astype(
        jnp.bfloat16
    )
    return influence[None]


def solution(mesh):
    layer_count = mesh.shape["layer"]
    fblk_count = mesh.shape["fblk"]
    split = Mesh(
        mesh.devices.reshape(LAYERS, layer_count // LAYERS, fblk_count), ("lg", "q", "fblk")
    )
    layer = ("lg", "q")
    in_specs = (P("fblk", layer), P("fblk", layer), P(None, layer), P(), P())
    out_specs = P(layer, "fblk", None)
    return jax.shard_map(
        on_device, mesh=split, in_specs=in_specs, out_specs=out_specs, check_vma=False
    )
```

```python
import jax
import jax.numpy as jnp
from jax import lax
from jax.experimental import pallas as pl
from jax.experimental.pallas import tpu as pltpu
from jax.sharding import Mesh
from jax.sharding import PartitionSpec as P

BLK = 512
ACTIVE_SLOTS = 3
LAYERS = 8
CHUNKS = 1
ROW_TILE = 64


def select_kernel(src_loc, tgt_loc, src_live, tgt_live, *refs):
    dec_refs = refs[:ACTIVE_SLOTS]
    enc_refs = refs[ACTIVE_SLOTS : 2 * ACTIVE_SLOTS]
    act_refs = refs[2 * ACTIVE_SLOTS : 3 * ACTIVE_SLOTS]
    out_ref = refs[3 * ACTIVE_SLOTS]
    prompt = pl.program_id(0)
    kind = pl.program_id(1)
    rows = dec_refs[0].shape[0]
    steps = rows // ROW_TILE

    @pl.when(kind == 0)
    def _():
        for slot in range(ACTIVE_SLOTS):
            weights = act_refs[slot][...].astype(jnp.float32)
            row = lax.broadcasted_iota(jnp.int32, weights.shape, 0)
            factor = jnp.sum(jnp.where(row == prompt, weights, 0.0), axis=0, keepdims=True)
            live = src_live[prompt, slot] > 0
            matrix_ref = dec_refs[slot]

            def body(index, carry, matrix_ref=matrix_ref, factor=factor, live=live, slot=slot):
                lower = pl.multiple_of(index * ROW_TILE, ROW_TILE)
                value = matrix_ref[pl.ds(lower, ROW_TILE), :].astype(jnp.float32) * factor
                out_ref[0, pl.ds(lower, ROW_TILE), pl.ds(slot * BLK, BLK)] = jnp.where(
                    live, value, 0.0
                ).astype(out_ref.dtype)
                return carry

            lax.fori_loop(0, steps, body, 0)

    @pl.when(kind == 1)
    def _():
        for slot in range(ACTIVE_SLOTS):
            live = tgt_live[prompt, slot] > 0
            matrix_ref = enc_refs[slot]

            def body(index, carry, matrix_ref=matrix_ref, live=live, slot=slot):
                lower = pl.multiple_of(index * ROW_TILE, ROW_TILE)
                value = matrix_ref[pl.ds(lower, ROW_TILE), :]
                out_ref[0, pl.ds(lower, ROW_TILE), pl.ds(slot * BLK, BLK)] = jnp.where(
                    live, value, jnp.zeros_like(value)
                )
                return carry

            lax.fori_loop(0, steps, body, 0)


def select_blocks(decoder, encoder, activation, src_loc, tgt_loc, src_live, tgt_live):
    rows, _ = decoder.shape
    prompts = activation.shape[0]
    slots = ACTIVE_SLOTS

    def held(loc, live, p, slot):
        block = loc[0, slot]
        for earlier in reversed(range(prompts)):
            block = jnp.where(live[earlier, slot] > 0, loc[earlier, slot], block)
        for earlier in range(prompts):
            block = jnp.where((earlier <= p) & (live[earlier, slot] > 0), loc[earlier, slot], block)
        return block

    def dec_map(slot):
        return lambda p, k, sl, tl, sv, tv: (0, held(sl, sv, p, slot))

    def enc_map(slot):
        return lambda p, k, sl, tl, sv, tv: (0, held(tl, tv, p, slot))

    def out_map(p, k, sl, tl, sv, tv):
        return (p, 0, k)

    grid_spec = pltpu.PrefetchScalarGridSpec(
        num_scalar_prefetch=4,
        grid=(prompts, 2),
        in_specs=[pl.BlockSpec((rows, BLK), dec_map(slot)) for slot in range(slots)]
        + [pl.BlockSpec((rows, BLK), enc_map(slot)) for slot in range(slots)]
        + [pl.BlockSpec((prompts, BLK), dec_map(slot)) for slot in range(slots)],
        out_specs=pl.BlockSpec((1, rows, slots * BLK), out_map),
    )
    block_bytes = rows * BLK * 2
    return pl.pallas_call(
        select_kernel,
        grid_spec=grid_spec,
        out_shape=jax.ShapeDtypeStruct((prompts, rows, 2 * slots * BLK), jnp.bfloat16),
        cost_estimate=pl.CostEstimate(
            flops=prompts * slots * rows * BLK,
            transcendentals=0,
            bytes_accessed=4 * prompts * slots * block_bytes,
        ),
    )(
        src_loc,
        tgt_loc,
        src_live,
        tgt_live,
        *([decoder] * slots),
        *([encoder] * slots),
        *([activation] * slots),
    )


def slot_tables(blocks, counts, layer, quarter, local_blocks):
    ids = lax.dynamic_index_in_dim(blocks, layer, 1, False)
    count = lax.dynamic_index_in_dim(counts, layer, 1, False)
    slot = jnp.arange(ids.shape[1], dtype=jnp.int32)[None, :]
    live = (slot < count[:, None]) & (ids // local_blocks == quarter)
    return (ids % local_blocks).astype(jnp.int32), live.astype(jnp.int32)


def on_device(decoder, encoder, activation, blocks, counts):
    group_count = lax.axis_size("lg")
    layer_group = lax.axis_index("lg")
    quarter = lax.axis_index("q")
    fblk = lax.axis_index("fblk")
    fblk_count = lax.axis_size("fblk")
    local_blocks = decoder.shape[1] // BLK
    active_width = ACTIVE_SLOTS * BLK
    share = active_width // fblk_count

    src_loc, src_live = slot_tables(blocks, counts, layer_group, quarter, local_blocks)
    tgt_loc, tgt_live = slot_tables(blocks, counts, layer_group + 1, quarter, local_blocks)
    combined = select_blocks(decoder, encoder, activation, src_loc, tgt_loc, src_live, tgt_live)
    combined = lax.psum_scatter(combined, "q", scatter_dimension=0, tiled=True)
    source = combined[0, :, :active_width]
    target = combined[0, :, active_width:]

    partial_gram = lax.dot_general(
        target, source, (((0,), (0,)), ((), ())), preferred_element_type=jnp.float32
    ).astype(jnp.bfloat16)
    gram_sum = lax.psum(partial_gram, "fblk").astype(jnp.float32)
    live_rows = (lax.dynamic_slice(counts, (quarter, layer_group), (1, 1))[0, 0] * BLK).astype(
        jnp.float32
    )
    row_mean = jnp.sum(jnp.abs(gram_sum), axis=1) / live_rows
    edges = (0.7 * gram_sum / ((row_mean[:, None] + 1e-06) * jnp.sqrt(live_rows))).astype(
        jnp.bfloat16
    )

    edges_t = edges.T
    mine = lax.dynamic_slice_in_dim(edges_t, fblk * share, share, 0)
    width = share // CHUNKS
    forward = [(index, index + 1) for index in range(group_count - 1)]
    for step in range(1, group_count + CHUNKS - 1):
        sent = jnp.clip(step - 1 - layer_group, 0, CHUNKS - 1)
        outgoing = lax.dynamic_slice_in_dim(mine, sent * width, width, 0)
        previous = lax.ppermute(outgoing, "lg", forward)
        product = jnp.dot(previous, edges_t, preferred_element_type=jnp.float32).astype(
            jnp.bfloat16
        )
        chunk = step - layer_group
        valid = (layer_group >= 1) & (chunk >= 0) & (chunk < CHUNKS)
        place = jnp.clip(chunk, 0, CHUNKS - 1)
        kept = lax.dynamic_slice_in_dim(mine, place * width, width, 0)
        mine = lax.dynamic_update_slice_in_dim(
            mine, jnp.where(valid, product, kept), place * width, 0
        )

    parts = []
    for shift in range(fblk_count):
        wanted = (fblk + shift) % fblk_count
        piece = lax.dynamic_slice_in_dim(mine, wanted * share, share, 1)
        if shift:
            pairs = [(index, (index + shift) % fblk_count) for index in range(fblk_count)]
            piece = lax.ppermute(piece, "fblk", pairs)
        parts.append(piece.T)
    ordered = [parts[(fblk_count - m) % fblk_count] for m in range(fblk_count)]
    doubled = jnp.concatenate(ordered + ordered, axis=1)
    rows = lax.dynamic_slice_in_dim(doubled, (fblk_count - fblk) * share, active_width, 1)
    influence = (jnp.sqrt(jnp.float32(active_width)) * rows.astype(jnp.float32)).astype(
        jnp.bfloat16
    )
    return influence[None]


def solution(mesh):
    layer_count = mesh.shape["layer"]
    fblk_count = mesh.shape["fblk"]
    split = Mesh(
        mesh.devices.reshape(LAYERS, layer_count // LAYERS, fblk_count), ("lg", "q", "fblk")
    )
    layer = ("lg", "q")
    in_specs = (P("fblk", layer), P("fblk", layer), P(None, layer), P(), P())
    out_specs = P(layer, "fblk", None)
    return jax.shard_map(
        on_device, mesh=split, in_specs=in_specs, out_specs=out_specs, check_vma=False
    )
```

```python
import jax
import jax.numpy as jnp
from jax import lax
from jax.experimental import pallas as pl
from jax.experimental.pallas import tpu as pltpu
from jax.sharding import Mesh
from jax.sharding import PartitionSpec as P

BLK = 512
ACTIVE_SLOTS = 3
LAYERS = 8
ROW_TILE = 64


def select_kernel(src_loc, tgt_loc, src_live, tgt_live, *refs):
    dec_refs = refs[:ACTIVE_SLOTS]
    enc_refs = refs[ACTIVE_SLOTS : 2 * ACTIVE_SLOTS]
    act_refs = refs[2 * ACTIVE_SLOTS : 3 * ACTIVE_SLOTS]
    out_ref = refs[3 * ACTIVE_SLOTS]
    prompt = pl.program_id(0)
    kind = pl.program_id(1)
    rows = dec_refs[0].shape[0]
    steps = rows // ROW_TILE

    @pl.when(kind == 0)
    def _():
        for slot in range(ACTIVE_SLOTS):
            weights = act_refs[slot][...].astype(jnp.float32)
            row = lax.broadcasted_iota(jnp.int32, weights.shape, 0)
            factor = jnp.sum(jnp.where(row == prompt, weights, 0.0), axis=0, keepdims=True)
            live = src_live[prompt, slot] > 0
            matrix_ref = dec_refs[slot]

            def body(index, carry, matrix_ref=matrix_ref, factor=factor, live=live, slot=slot):
                lower = pl.multiple_of(index * ROW_TILE, ROW_TILE)
                value = matrix_ref[pl.ds(lower, ROW_TILE), :].astype(jnp.float32) * factor
                out_ref[0, pl.ds(lower, ROW_TILE), pl.ds(slot * BLK, BLK)] = jnp.where(
                    live, value, 0.0
                ).astype(out_ref.dtype)
                return carry

            lax.fori_loop(0, steps, body, 0)

    @pl.when(kind == 1)
    def _():
        for slot in range(ACTIVE_SLOTS):
            live = tgt_live[prompt, slot] > 0
            matrix_ref = enc_refs[slot]

            def body(index, carry, matrix_ref=matrix_ref, live=live, slot=slot):
                lower = pl.multiple_of(index * ROW_TILE, ROW_TILE)
                value = matrix_ref[pl.ds(lower, ROW_TILE), :]
                out_ref[0, pl.ds(lower, ROW_TILE), pl.ds(slot * BLK, BLK)] = jnp.where(
                    live, value, jnp.zeros_like(value)
                )
                return carry

            lax.fori_loop(0, steps, body, 0)


def select_blocks(decoder, encoder, activation, src_loc, tgt_loc, src_live, tgt_live):
    rows, _ = decoder.shape
    prompts = activation.shape[0]
    slots = ACTIVE_SLOTS

    def held(loc, live, p, slot):
        block = loc[0, slot]
        for earlier in reversed(range(prompts)):
            block = jnp.where(live[earlier, slot] > 0, loc[earlier, slot], block)
        for earlier in range(prompts):
            block = jnp.where((earlier <= p) & (live[earlier, slot] > 0), loc[earlier, slot], block)
        return block

    def dec_map(slot):
        return lambda p, k, sl, tl, sv, tv: (0, held(sl, sv, p, slot))

    def enc_map(slot):
        return lambda p, k, sl, tl, sv, tv: (0, held(tl, tv, p, slot))

    def out_map(p, k, sl, tl, sv, tv):
        return (p, 0, k)

    grid_spec = pltpu.PrefetchScalarGridSpec(
        num_scalar_prefetch=4,
        grid=(prompts, 2),
        in_specs=[pl.BlockSpec((rows, BLK), dec_map(slot)) for slot in range(slots)]
        + [pl.BlockSpec((rows, BLK), enc_map(slot)) for slot in range(slots)]
        + [pl.BlockSpec((prompts, BLK), dec_map(slot)) for slot in range(slots)],
        out_specs=pl.BlockSpec((1, rows, slots * BLK), out_map),
    )
    block_bytes = rows * BLK * 2
    return pl.pallas_call(
        select_kernel,
        grid_spec=grid_spec,
        out_shape=jax.ShapeDtypeStruct((prompts, rows, 2 * slots * BLK), jnp.bfloat16),
        cost_estimate=pl.CostEstimate(
            flops=prompts * slots * rows * BLK,
            transcendentals=0,
            bytes_accessed=4 * prompts * slots * block_bytes,
        ),
    )(
        src_loc,
        tgt_loc,
        src_live,
        tgt_live,
        *([decoder] * slots),
        *([encoder] * slots),
        *([activation] * slots),
    )


def slot_tables(blocks, counts, layer, quarter, local_blocks):
    ids = lax.dynamic_index_in_dim(blocks, layer, 1, False)
    count = lax.dynamic_index_in_dim(counts, layer, 1, False)
    slot = jnp.arange(ids.shape[1], dtype=jnp.int32)[None, :]
    live = (slot < count[:, None]) & (ids // local_blocks == quarter)
    return (ids % local_blocks).astype(jnp.int32), live.astype(jnp.int32)


def on_device(decoder, encoder, activation, blocks, counts):
    group_count = lax.axis_size("lg")
    layer_group = lax.axis_index("lg")
    quarter = lax.axis_index("q")
    fblk = lax.axis_index("fblk")
    fblk_count = lax.axis_size("fblk")
    local_blocks = decoder.shape[1] // BLK
    active_width = ACTIVE_SLOTS * BLK
    share = active_width // fblk_count

    src_loc, src_live = slot_tables(blocks, counts, layer_group, quarter, local_blocks)
    tgt_loc, tgt_live = slot_tables(blocks, counts, layer_group + 1, quarter, local_blocks)
    combined = select_blocks(decoder, encoder, activation, src_loc, tgt_loc, src_live, tgt_live)
    combined = lax.psum_scatter(combined, "q", scatter_dimension=0, tiled=True)
    source = combined[0, :, :active_width]
    target = combined[0, :, active_width:]

    partial_gram = lax.dot_general(
        target, source, (((0,), (0,)), ((), ())), preferred_element_type=jnp.float32
    ).astype(jnp.bfloat16)
    gram_sum = lax.psum(partial_gram, "fblk").astype(jnp.float32)
    live_rows = (lax.dynamic_slice(counts, (quarter, layer_group), (1, 1))[0, 0] * BLK).astype(
        jnp.float32
    )
    row_mean = jnp.sum(jnp.abs(gram_sum), axis=1) / live_rows
    edges = (0.7 * gram_sum / ((row_mean[:, None] + 1e-06) * jnp.sqrt(live_rows))).astype(
        jnp.bfloat16
    )

    mine = lax.dynamic_slice_in_dim(edges, fblk * share, share, 1)
    forward = [(index, index + 1) for index in range(group_count - 1)]
    for step in range(1, group_count):
        previous = lax.ppermute(mine, "lg", forward)
        product = jnp.dot(edges, previous, preferred_element_type=jnp.float32).astype(
            jnp.bfloat16
        )
        mine = jnp.where(layer_group == step, product, mine)

    parts = []
    for shift in range(fblk_count):
        wanted = (fblk + shift) % fblk_count
        piece = lax.dynamic_slice_in_dim(mine, wanted * share, share, 0)
        if shift:
            pairs = [(index, (index + shift) % fblk_count) for index in range(fblk_count)]
            piece = lax.ppermute(piece, "fblk", pairs)
        parts.append(piece)
    ordered = [parts[(fblk_count - m) % fblk_count] for m in range(fblk_count)]
    doubled = jnp.concatenate(ordered + ordered, axis=1)
    rows = lax.dynamic_slice_in_dim(doubled, (fblk_count - fblk) * share, active_width, 1)
    influence = (jnp.sqrt(jnp.float32(active_width)) * rows.astype(jnp.float32)).astype(
        jnp.bfloat16
    )
    return influence[None]


def solution(mesh):
    layer_count = mesh.shape["layer"]
    fblk_count = mesh.shape["fblk"]
    split = Mesh(
        mesh.devices.reshape(LAYERS, layer_count // LAYERS, fblk_count), ("lg", "q", "fblk")
    )
    layer = ("lg", "q")
    in_specs = (P("fblk", layer), P("fblk", layer), P(None, layer), P(), P())
    out_specs = P(layer, "fblk", None)
    return jax.shard_map(
        on_device, mesh=split, in_specs=in_specs, out_specs=out_specs, check_vma=False
    )
```

```python
import jax
import jax.numpy as jnp
from jax import lax
from jax.experimental import pallas as pl
from jax.experimental.pallas import tpu as pltpu
from jax.sharding import Mesh
from jax.sharding import PartitionSpec as P

BLK = 512
ACTIVE_SLOTS = 3
LAYERS = 8
ROW_TILE = 192


def select_kernel(src_loc, tgt_loc, src_live, tgt_live, *refs):
    dec_refs = refs[:ACTIVE_SLOTS]
    enc_refs = refs[ACTIVE_SLOTS : 2 * ACTIVE_SLOTS]
    act_refs = refs[2 * ACTIVE_SLOTS : 3 * ACTIVE_SLOTS]
    out_ref = refs[3 * ACTIVE_SLOTS]
    prompt = pl.program_id(0)
    kind = pl.program_id(1)
    rows = dec_refs[0].shape[0]
    steps = rows // ROW_TILE

    @pl.when(kind == 0)
    def _():
        for slot in range(ACTIVE_SLOTS):
            weights = act_refs[slot][...].astype(jnp.float32)
            row = lax.broadcasted_iota(jnp.int32, weights.shape, 0)
            factor = jnp.sum(jnp.where(row == prompt, weights, 0.0), axis=0, keepdims=True)
            live = src_live[prompt, slot] > 0
            matrix_ref = dec_refs[slot]

            def body(index, carry, matrix_ref=matrix_ref, factor=factor, live=live, slot=slot):
                lower = pl.multiple_of(index * ROW_TILE, ROW_TILE)
                value = matrix_ref[pl.ds(lower, ROW_TILE), :].astype(jnp.float32) * factor
                out_ref[0, pl.ds(lower, ROW_TILE), pl.ds(slot * BLK, BLK)] = jnp.where(
                    live, value, 0.0
                ).astype(out_ref.dtype)
                return carry

            lax.fori_loop(0, steps, body, 0)

    @pl.when(kind == 1)
    def _():
        for slot in range(ACTIVE_SLOTS):
            live = tgt_live[prompt, slot] > 0
            matrix_ref = enc_refs[slot]

            def body(index, carry, matrix_ref=matrix_ref, live=live, slot=slot):
                lower = pl.multiple_of(index * ROW_TILE, ROW_TILE)
                value = matrix_ref[pl.ds(lower, ROW_TILE), :]
                out_ref[0, pl.ds(lower, ROW_TILE), pl.ds(slot * BLK, BLK)] = jnp.where(
                    live, value, jnp.zeros_like(value)
                )
                return carry

            lax.fori_loop(0, steps, body, 0)


def select_blocks(decoder, encoder, activation, src_loc, tgt_loc, src_live, tgt_live):
    rows, _ = decoder.shape
    prompts = activation.shape[0]
    slots = ACTIVE_SLOTS

    def held(loc, live, p, slot):
        block = loc[0, slot]
        for earlier in reversed(range(prompts)):
            block = jnp.where(live[earlier, slot] > 0, loc[earlier, slot], block)
        for earlier in range(prompts):
            block = jnp.where((earlier <= p) & (live[earlier, slot] > 0), loc[earlier, slot], block)
        return block

    def dec_map(slot):
        return lambda p, k, sl, tl, sv, tv: (0, held(sl, sv, p, slot))

    def enc_map(slot):
        return lambda p, k, sl, tl, sv, tv: (0, held(tl, tv, p, slot))

    def out_map(p, k, sl, tl, sv, tv):
        return (p, 0, k)

    grid_spec = pltpu.PrefetchScalarGridSpec(
        num_scalar_prefetch=4,
        grid=(prompts, 2),
        in_specs=[pl.BlockSpec((rows, BLK), dec_map(slot)) for slot in range(slots)]
        + [pl.BlockSpec((rows, BLK), enc_map(slot)) for slot in range(slots)]
        + [pl.BlockSpec((prompts, BLK), dec_map(slot)) for slot in range(slots)],
        out_specs=pl.BlockSpec((1, rows, slots * BLK), out_map),
    )
    block_bytes = rows * BLK * 2
    return pl.pallas_call(
        select_kernel,
        grid_spec=grid_spec,
        out_shape=jax.ShapeDtypeStruct((prompts, rows, 2 * slots * BLK), jnp.bfloat16),
        cost_estimate=pl.CostEstimate(
            flops=prompts * slots * rows * BLK,
            transcendentals=0,
            bytes_accessed=4 * prompts * slots * block_bytes,
        ),
    )(
        src_loc,
        tgt_loc,
        src_live,
        tgt_live,
        *([decoder] * slots),
        *([encoder] * slots),
        *([activation] * slots),
    )


def slot_tables(blocks, counts, layer, quarter, local_blocks):
    ids = lax.dynamic_index_in_dim(blocks, layer, 1, False)
    count = lax.dynamic_index_in_dim(counts, layer, 1, False)
    slot = jnp.arange(ids.shape[1], dtype=jnp.int32)[None, :]
    live = (slot < count[:, None]) & (ids // local_blocks == quarter)
    return (ids % local_blocks).astype(jnp.int32), live.astype(jnp.int32)


def on_device(decoder, encoder, activation, blocks, counts):
    group_count = lax.axis_size("lg")
    layer_group = lax.axis_index("lg")
    quarter = lax.axis_index("q")
    fblk = lax.axis_index("fblk")
    fblk_count = lax.axis_size("fblk")
    local_blocks = decoder.shape[1] // BLK
    active_width = ACTIVE_SLOTS * BLK
    share = active_width // fblk_count

    src_loc, src_live = slot_tables(blocks, counts, layer_group, quarter, local_blocks)
    tgt_loc, tgt_live = slot_tables(blocks, counts, layer_group + 1, quarter, local_blocks)
    combined = select_blocks(decoder, encoder, activation, src_loc, tgt_loc, src_live, tgt_live)
    combined = lax.psum_scatter(combined, "q", scatter_dimension=0, tiled=True)
    source = combined[0, :, :active_width]
    target = combined[0, :, active_width:]

    partial_gram = lax.dot_general(
        target, source, (((0,), (0,)), ((), ())), preferred_element_type=jnp.float32
    ).astype(jnp.bfloat16)
    gram_sum = lax.psum(partial_gram, "fblk").astype(jnp.float32)
    live_rows = (lax.dynamic_slice(counts, (quarter, layer_group), (1, 1))[0, 0] * BLK).astype(
        jnp.float32
    )
    row_mean = jnp.sum(jnp.abs(gram_sum), axis=1) / live_rows
    edges = (0.7 * gram_sum / ((row_mean[:, None] + 1e-06) * jnp.sqrt(live_rows))).astype(
        jnp.bfloat16
    )

    mine = lax.dynamic_slice_in_dim(edges, fblk * share, share, 1)
    forward = [(index, index + 1) for index in range(group_count - 1)]
    for step in range(1, group_count):
        previous = lax.ppermute(mine, "lg", forward)
        product = jnp.dot(edges, previous, preferred_element_type=jnp.float32).astype(
            jnp.bfloat16
        )
        mine = jnp.where(layer_group == step, product, mine)

    parts = []
    for shift in range(fblk_count):
        wanted = (fblk + shift) % fblk_count
        piece = lax.dynamic_slice_in_dim(mine, wanted * share, share, 0)
        if shift:
            pairs = [(index, (index + shift) % fblk_count) for index in range(fblk_count)]
            piece = lax.ppermute(piece, "fblk", pairs)
        parts.append(piece)
    ordered = [parts[(fblk_count - m) % fblk_count] for m in range(fblk_count)]
    doubled = jnp.concatenate(ordered + ordered, axis=1)
    rows = lax.dynamic_slice_in_dim(doubled, (fblk_count - fblk) * share, active_width, 1)
    influence = (jnp.sqrt(jnp.float32(active_width)) * rows.astype(jnp.float32)).astype(
        jnp.bfloat16
    )
    return influence[None]


def solution(mesh):
    layer_count = mesh.shape["layer"]
    fblk_count = mesh.shape["fblk"]
    split = Mesh(
        mesh.devices.reshape(LAYERS, layer_count // LAYERS, fblk_count), ("lg", "q", "fblk")
    )
    layer = ("lg", "q")
    in_specs = (P("fblk", layer), P("fblk", layer), P(None, layer), P(), P())
    out_specs = P(layer, "fblk", None)
    return jax.shard_map(
        on_device, mesh=split, in_specs=in_specs, out_specs=out_specs, check_vma=False
    )
```

```python
import jax
import jax.numpy as jnp
from jax import lax
from jax.experimental import pallas as pl
from jax.experimental.pallas import tpu as pltpu
from jax.sharding import Mesh
from jax.sharding import PartitionSpec as P

BLK = 512
ACTIVE_SLOTS = 3
LAYERS = 8
ROW_TILE = 64


def select_kernel(src_loc, tgt_loc, src_live, tgt_live, *refs):
    dec_refs = refs[:ACTIVE_SLOTS]
    enc_refs = refs[ACTIVE_SLOTS : 2 * ACTIVE_SLOTS]
    act_refs = refs[2 * ACTIVE_SLOTS : 3 * ACTIVE_SLOTS]
    out_ref = refs[3 * ACTIVE_SLOTS]
    prompt = pl.program_id(0)
    kind = pl.program_id(1)
    rows = dec_refs[0].shape[0]
    steps = rows // ROW_TILE

    @pl.when(kind == 0)
    def _():
        for slot in range(ACTIVE_SLOTS):
            weights = act_refs[slot][...].astype(jnp.float32)
            row = lax.broadcasted_iota(jnp.int32, weights.shape, 0)
            factor = jnp.sum(jnp.where(row == prompt, weights, 0.0), axis=0, keepdims=True)
            live = src_live[prompt, slot] > 0
            matrix_ref = dec_refs[slot]

            def body(index, carry, matrix_ref=matrix_ref, factor=factor, live=live, slot=slot):
                lower = pl.multiple_of(index * ROW_TILE, ROW_TILE)
                value = matrix_ref[pl.ds(lower, ROW_TILE), :].astype(jnp.float32) * factor
                out_ref[0, pl.ds(lower, ROW_TILE), pl.ds(slot * BLK, BLK)] = jnp.where(
                    live, value, 0.0
                ).astype(out_ref.dtype)
                return carry

            lax.fori_loop(0, steps, body, 0)

    @pl.when(kind == 1)
    def _():
        for slot in range(ACTIVE_SLOTS):
            live = tgt_live[prompt, slot] > 0
            matrix_ref = enc_refs[slot]

            def body(index, carry, matrix_ref=matrix_ref, live=live, slot=slot):
                lower = pl.multiple_of(index * ROW_TILE, ROW_TILE)
                value = matrix_ref[pl.ds(lower, ROW_TILE), :]
                out_ref[0, pl.ds(lower, ROW_TILE), pl.ds(slot * BLK, BLK)] = jnp.where(
                    live, value, jnp.zeros_like(value)
                )
                return carry

            lax.fori_loop(0, steps, body, 0)


def select_blocks(decoder, encoder, activation, src_loc, tgt_loc, src_live, tgt_live):
    rows, _ = decoder.shape
    prompts = activation.shape[0]
    slots = ACTIVE_SLOTS

    def held(loc, live, p, slot):
        block = loc[0, slot]
        for earlier in reversed(range(prompts)):
            block = jnp.where(live[earlier, slot] > 0, loc[earlier, slot], block)
        for earlier in range(prompts):
            block = jnp.where((earlier <= p) & (live[earlier, slot] > 0), loc[earlier, slot], block)
        return block

    def dec_map(slot):
        return lambda p, k, sl, tl, sv, tv: (0, held(sl, sv, p, slot))

    def enc_map(slot):
        return lambda p, k, sl, tl, sv, tv: (0, held(tl, tv, p, slot))

    def out_map(p, k, sl, tl, sv, tv):
        return (p, 0, k)

    grid_spec = pltpu.PrefetchScalarGridSpec(
        num_scalar_prefetch=4,
        grid=(prompts, 2),
        in_specs=[pl.BlockSpec((rows, BLK), dec_map(slot)) for slot in range(slots)]
        + [pl.BlockSpec((rows, BLK), enc_map(slot)) for slot in range(slots)]
        + [pl.BlockSpec((prompts, BLK), dec_map(slot)) for slot in range(slots)],
        out_specs=pl.BlockSpec((1, rows, slots * BLK), out_map),
    )
    block_bytes = rows * BLK * 2
    return pl.pallas_call(
        select_kernel,
        grid_spec=grid_spec,
        out_shape=jax.ShapeDtypeStruct((prompts, rows, 2 * slots * BLK), jnp.bfloat16),
        cost_estimate=pl.CostEstimate(
            flops=prompts * slots * rows * BLK,
            transcendentals=0,
            bytes_accessed=4 * prompts * slots * block_bytes,
        ),
    )(
        src_loc,
        tgt_loc,
        src_live,
        tgt_live,
        *([decoder] * slots),
        *([encoder] * slots),
        *([activation] * slots),
    )


def slot_tables(blocks, counts, layer, quarter, local_blocks):
    ids = lax.dynamic_index_in_dim(blocks, layer, 1, False)
    count = lax.dynamic_index_in_dim(counts, layer, 1, False)
    slot = jnp.arange(ids.shape[1], dtype=jnp.int32)[None, :]
    live = (slot < count[:, None]) & (ids // local_blocks == quarter)
    return (ids % local_blocks).astype(jnp.int32), live.astype(jnp.int32)


def on_device(decoder, encoder, activation, blocks, counts):
    group_count = lax.axis_size("lg")
    layer_group = lax.axis_index("lg")
    quarter = lax.axis_index("q")
    fblk = lax.axis_index("fblk")
    fblk_count = lax.axis_size("fblk")
    local_blocks = decoder.shape[1] // BLK
    active_width = ACTIVE_SLOTS * BLK
    share = active_width // fblk_count

    src_loc, src_live = slot_tables(blocks, counts, layer_group, quarter, local_blocks)
    tgt_loc, tgt_live = slot_tables(blocks, counts, layer_group + 1, quarter, local_blocks)
    combined = select_blocks(decoder, encoder, activation, src_loc, tgt_loc, src_live, tgt_live)
    combined = lax.psum_scatter(combined, "q", scatter_dimension=0, tiled=True)
    source = combined[0, :, :active_width]
    target = combined[0, :, active_width:]

    partial_gram = lax.dot_general(
        target, source, (((0,), (0,)), ((), ())), preferred_element_type=jnp.float32
    ).astype(jnp.bfloat16)
    gram_sum = lax.psum(partial_gram, "fblk").astype(jnp.float32)
    live_rows = (lax.dynamic_slice(counts, (quarter, layer_group), (1, 1))[0, 0] * BLK).astype(
        jnp.float32
    )
    row_mean = jnp.sum(jnp.abs(gram_sum), axis=1) / live_rows
    edges = (0.7 * gram_sum / ((row_mean[:, None] + 1e-06) * jnp.sqrt(live_rows))).astype(
        jnp.bfloat16
    )

    mine = lax.dynamic_slice_in_dim(edges, fblk * share, share, 1)
    forward = [(index, index + 1) for index in range(group_count - 1)]
    for step in range(1, group_count):
        previous = lax.ppermute(mine, "lg", forward)
        product = jnp.dot(edges, previous, preferred_element_type=jnp.float32).astype(
            jnp.bfloat16
        )
        mine = jnp.where(layer_group == step, product, mine)

    rows = lax.all_to_all(mine, "fblk", 0, 1, tiled=True)
    influence = (jnp.sqrt(jnp.float32(active_width)) * rows.astype(jnp.float32)).astype(
        jnp.bfloat16
    )
    return influence[None]


def solution(mesh):
    layer_count = mesh.shape["layer"]
    fblk_count = mesh.shape["fblk"]
    split = Mesh(
        mesh.devices.reshape(LAYERS, layer_count // LAYERS, fblk_count), ("lg", "q", "fblk")
    )
    layer = ("lg", "q")
    in_specs = (P("fblk", layer), P("fblk", layer), P(None, layer), P(), P())
    out_specs = P(layer, "fblk", None)
    return jax.shard_map(
        on_device, mesh=split, in_specs=in_specs, out_specs=out_specs, check_vma=False
    )
```
